128 devices in a mesh: expo: 8 (over z, core), sky: 16 (over x, y).
Axes of the slice: x: 4, y: 4, z: 4, core: 2. Of those that a mesh axis runs over, the one named last changes fastest.
Arguments:
- samples: bfloat16 [1024, 32, 256], P('sky'), may hold values from -0.75 to 0.75
- basis: bfloat16 [256, 1024], replicated, may hold values from -3 to 3
- operators: bfloat16 [1024, 1024, 1024], P(('expo', 'sky')), may hold values from -0.1875 to 0.1875
- cutouts: float32 [1024, 16, 1024], P(('expo', 'sky')), may hold values from -6 to 6
- pixel_weights: float32 [1024, 16, 1024], P(('expo', 'sky')), may hold values from 0.25 to 4
- detections: int32 [8, 16, 16, 12], P('expo', 'sky'), may hold values from -1 to 63, as said below
- intersections: int32 [1024, 16], P(('expo', 'sky')), may hold values from -1 to 191, as said below
Outputs:
- loglik: float32 [1024, 32], P('sky', 'expo')
- coeff_grads: float32 [1024, 32, 256], P('sky', 'expo')
The draws below stay inside these ranges and needn't reach their ends.
Inputs may be any that keep to these rules, and one draw needn't show every extreme that they name: In detections[e, s, c], the live slots (values 0 or more) come first; -1 marks the rest. For every device (e, c), the live slots over all s total exactly 96, and one s fills all 12. A galaxy may stand in several slots. `intersections`: on device (e, c), a slot r = s * 12 + j is live exactly when detections[e, s, c, j] >= 0, and each live slot stands at exactly one position of the device's tiles; -1 marks empty positions. One tile of every device has all 16 positions filled.
All inputs are finite; a program needn't handle non-finite values.
Results may differ from the reference program's by a relative error of at most 0.0017.
Values may be sent and summed in bfloat16 or wider, within the bound.
No kernel may reach another device: no remote copies, remote signals or barrier semaphores. Data moves between devices by JAX's collectives and lax.ppermute only.
A program may use at most 128 MiB of HBM per device.

```python
import math
import jax
import jax.numpy as jnp
from jax import lax

K = 256
P_SIZE = 1024
S = 32
G_DEV = 64
PAIR_DEV = 96
TILE_DEV = 8
TCAP = 16
CAP = 12
GAL = 1024
TILES = 1024
N_EXPO = 8
N_SKY = 16


def plan_device(key):
    keys = jax.random.split(key, 6)
    full_source = jax.random.randint(keys[0], (), 0, N_SKY)
    chosen = jax.random.permutation(keys[1], (N_SKY - 1) * CAP) < PAIR_DEV - CAP
    other_counts = jnp.sum(chosen.reshape(N_SKY - 1, CAP).astype(jnp.int32), axis=1)
    sources = jnp.arange(N_SKY, dtype=jnp.int32)
    pick = jnp.clip(sources - (sources > full_source).astype(jnp.int32), 0, N_SKY - 2)
    counts = jnp.where(sources == full_source, CAP, other_counts[pick])
    live = jnp.arange(CAP, dtype=jnp.int32)[None, :] < counts[:, None]
    galaxy = jax.random.randint(keys[2], (N_SKY, CAP), 0, G_DEV)
    listed = jnp.where(live, galaxy, -1).astype(jnp.int32)
    full_tile = jax.random.randint(keys[3], (), 0, TILE_DEV)
    filled_other = jax.random.permutation(keys[4], (TILE_DEV - 1) * TCAP) < PAIR_DEV - TCAP
    tile_numbers = jnp.arange(TILE_DEV, dtype=jnp.int32)
    tile_pick = jnp.clip(tile_numbers - (tile_numbers > full_tile).astype(jnp.int32), 0, TILE_DEV - 2)
    filled = jnp.where((tile_numbers == full_tile)[:, None], True, filled_other.reshape(TILE_DEV - 1, TCAP)[tile_pick])
    slot_numbers = jnp.arange(N_SKY * CAP, dtype=jnp.int32)
    order = jnp.argsort(jnp.where(live.reshape(-1), slot_numbers, slot_numbers + N_SKY * CAP), stable=True)[:PAIR_DEV]
    order = order[jax.random.permutation(keys[5], PAIR_DEV)]
    position_numbers = jnp.arange(TILE_DEV * TCAP, dtype=jnp.int32)
    position_order = jnp.argsort(jnp.where(filled.reshape(-1), position_numbers, position_numbers + TILE_DEV * TCAP), stable=True)[:PAIR_DEV]
    placed = jnp.full((TILE_DEV * TCAP,), -1, jnp.int32).at[position_order].set(order.astype(jnp.int32))
    return (listed, placed.reshape(TILE_DEV, TCAP))


def plan_all(key):
    keys = jax.random.split(jax.random.fold_in(key, 11), N_EXPO * N_SKY)
    return jax.vmap(plan_device)(keys)


def draw_detections(key, part):
    listed, placed = plan_all(key)
    return listed.reshape(N_EXPO, N_SKY, N_SKY, CAP).transpose(0, 2, 1, 3)


def draw_intersections(key, part):
    listed, placed = plan_all(key)
    return placed.reshape(TILES, TCAP)


def shard_levels(rng, dims, pieces, least, top_value):
    level = 1.0
    for dim, blocks in pieces:
        heights = jax.random.uniform(jax.random.fold_in(jax.random.fold_in(rng, 6), dim), (blocks,), jnp.float32, least / len(pieces), top_value / len(pieces))
        level = level * jnp.repeat(jnp.exp(heights), dims[dim] // blocks).reshape((-1,) + (1,) * (len(dims) - 1 - dim))
    return level


def noise(rng, extent, width, limit, pieces=(), kind=jnp.bfloat16):
    loudness = shard_levels(rng, extent, pieces, -0.22, 0.18) if pieces else 1.0
    values = jax.random.normal(rng, extent, jnp.float32) * width * loudness
    return jnp.minimum(jnp.maximum(values, -limit), limit).astype(kind)


def setup_inputs(seed: int = 0) -> dict:
    streams_of = jax.random.split(jax.random.key(seed), 8)
    return {
        "samples": noise(streams_of[0], (GAL, S, K), 0.125, 0.75, ((0, 16),)),
        "basis": noise(streams_of[1], (K, P_SIZE), 0.5, 3.0),
        "operators": noise(streams_of[2], (TILES, P_SIZE, P_SIZE), P_SIZE ** -0.5, 0.1875, ((0, 128),)),
        "cutouts": noise(streams_of[3], (TILES, TCAP, P_SIZE), 1.0, 6.0, ((0, 128),), jnp.float32),
        "pixel_weights": jnp.clip(jnp.exp(math.log(4.0) - 2.7725887 * jax.random.uniform(streams_of[4], (TILES, TCAP, P_SIZE), jnp.float32) ** shard_levels(streams_of[4], (TILES, TCAP, P_SIZE), ((0, 128),), -0.2, 0.2)), 0.25, 4.0),
        "detections": draw_detections(jax.random.fold_in(streams_of[7], 71), 0),
        "intersections": draw_intersections(jax.random.fold_in(streams_of[7], 71), 0),
    }


def reference(samples, basis, operators, cutouts, pixel_weights, detections, intersections):
    flat_samples = samples.reshape(GAL, S * K)
    basis_f = basis.astype(jnp.float32)

    def device_step(carry, device):
        grad_acc, like_acc = carry
        row = device // N_SKY
        column = device % N_SKY
        tile_ops = lax.dynamic_slice_in_dim(operators, device * TILE_DEV, TILE_DEV, 0).astype(jnp.float32)
        tile_data = lax.dynamic_slice_in_dim(cutouts, device * TILE_DEV, TILE_DEV, 0)
        tile_weights = lax.dynamic_slice_in_dim(pixel_weights, device * TILE_DEV, TILE_DEV, 0)
        listed = lax.dynamic_slice_in_dim(intersections, device * TILE_DEV, TILE_DEV, 0)
        live = listed >= 0
        slot = jnp.maximum(listed, 0)
        source = slot // CAP
        within = slot % CAP
        local_gal = detections[row, source, column, within]
        galaxy = source * G_DEV + local_gal
        picked = flat_samples[jnp.where(live, galaxy, 0)].reshape(-1, K)
        rendered = jnp.dot(picked, basis, preferred_element_type=jnp.float32).astype(jnp.bfloat16)
        rendered = rendered.reshape(TILE_DEV, TCAP * S, P_SIZE).astype(jnp.float32)
        model = jnp.einsum("tnp,tpq->tnq", rendered, tile_ops).reshape(TILE_DEV, TCAP, S, P_SIZE)
        resid = model - tile_data[:, :, None, :]
        weighted = tile_weights[:, :, None, :] * resid
        pair_like = (-0.5 / P_SIZE) * jnp.sum(weighted * resid, axis=-1)
        scaled = weighted.astype(jnp.bfloat16).reshape(TILE_DEV, TCAP * S, P_SIZE).astype(jnp.float32)
        backed = jnp.einsum("tnq,tpq->tnp", scaled, tile_ops).astype(jnp.bfloat16).astype(jnp.float32)
        pair_grad = (-1.0 / P_SIZE) * jnp.einsum("np,kp->nk", backed.reshape(-1, P_SIZE), basis_f)
        target = jnp.where(live, galaxy, GAL).reshape(-1)
        grad_acc = grad_acc.at[target].add(pair_grad.reshape(TILE_DEV * TCAP, S * K), mode="drop")
        like_acc = like_acc.at[target].add(pair_like.reshape(TILE_DEV * TCAP, S), mode="drop")
        return (grad_acc, like_acc), None

    start = (jnp.zeros((GAL, S * K), jnp.float32), jnp.zeros((GAL, S), jnp.float32))
    (grad_acc, like_acc), _ = lax.scan(device_step, start, jnp.arange(N_EXPO * N_SKY, dtype=jnp.int32))
    return (like_acc, grad_acc.reshape(GAL, S, K))
```

```python
import jax
import jax.numpy as jnp
from jax import lax
from jax.sharding import PartitionSpec as P

N_CHUNKS = 2
LANE = 128


def galaxy_sums(listed, values, galaxy_count):
    flat_list = listed.reshape(-1)
    onehot = (flat_list[None, :] == jnp.arange(galaxy_count, dtype=jnp.int32)[:, None]).astype(
        jnp.float32
    )
    return jnp.dot(onehot, values.reshape(flat_list.shape[0], -1), precision=lax.Precision.HIGHEST)


def per_device(samples, basis, operators, cutouts, pixel_weights, detections, intersections):
    tiles_here, tile_cap, pixels = cutouts.shape
    coeff_dim = basis.shape[0]
    galaxy_count, sample_count, _unused = samples.shape
    sky_count = lax.axis_size("sky")
    expo_count = lax.axis_size("expo")
    send_cap = detections.shape[3]
    slot_count = sky_count * send_cap
    per_expo = sample_count // expo_count
    chunk_size = per_expo // N_CHUNKS
    chunk_samples = expo_count * chunk_size
    sent_rows = detections.reshape(sky_count, send_cap)
    positions = tiles_here * tile_cap

    outgoing = jnp.take(samples, jnp.maximum(sent_rows, 0), axis=0)
    outgoing = outgoing.reshape(sky_count, send_cap, expo_count, N_CHUNKS, chunk_size, coeff_dim)
    live = intersections >= 0
    pick = jnp.maximum(intersections, 0).reshape(-1)
    target = jnp.where(live, intersections, slot_count).reshape(-1)
    grad_width = chunk_samples * coeff_dim
    width = grad_width + LANE

    grad_pieces = []
    like_pieces = []
    for chunk in range(N_CHUNKS):
        sent = outgoing[:, :, :, chunk].reshape(sky_count, send_cap, chunk_samples * coeff_dim)
        incoming = lax.all_to_all(sent, "sky", split_axis=0, concat_axis=0, tiled=True)
        incoming = incoming.reshape(slot_count, chunk_samples * coeff_dim)
        picked = jnp.take(incoming, pick, axis=0).reshape(-1, coeff_dim)
        rendered = jnp.dot(picked, basis, preferred_element_type=jnp.float32).astype(jnp.bfloat16)
        rendered = rendered.reshape(tiles_here, tile_cap * chunk_samples, pixels)
        model = jnp.einsum("tnp,tpq->tnq", rendered, operators, preferred_element_type=jnp.float32)
        model = model.reshape(tiles_here, tile_cap, chunk_samples, pixels)
        resid = model - cutouts[:, :, None, :]
        weighted = pixel_weights[:, :, None, :] * resid
        pair_like = -0.5 / pixels * jnp.sum(weighted * resid, axis=-1)
        scaled = weighted.astype(jnp.bfloat16).reshape(tiles_here, tile_cap * chunk_samples, pixels)
        backed = jnp.einsum(
            "tnq,tpq->tnp", scaled, operators, preferred_element_type=jnp.float32
        ).astype(jnp.bfloat16)
        pair_grad = (
            -1.0
            / pixels
            * lax.dot_general(
                backed.reshape(-1, pixels),
                basis,
                (((1,), (1,)), ((), ())),
                preferred_element_type=jnp.float32,
            )
        )
        payload = jnp.concatenate(
            [
                pair_grad.reshape(positions, grad_width),
                pair_like.reshape(positions, chunk_samples),
                jnp.zeros((positions, LANE - chunk_samples), jnp.float32),
            ],
            axis=1,
        )
        slot_payload = jnp.zeros((slot_count, width), jnp.float32)
        slot_payload = slot_payload.at[target].set(payload, mode="drop")
        back = lax.all_to_all(
            slot_payload.reshape(sky_count, send_cap, width),
            "sky",
            split_axis=0,
            concat_axis=0,
            tiled=True,
        )
        summed = galaxy_sums(sent_rows, back, galaxy_count)
        grads = summed[:, :grad_width].reshape(galaxy_count, expo_count, chunk_size * coeff_dim)
        likes = summed[:, grad_width : grad_width + chunk_samples].reshape(
            galaxy_count, expo_count, chunk_size
        )
        like_rows = likes.transpose(1, 2, 0).reshape(1, chunk_samples, galaxy_count)
        flat = jnp.concatenate(
            [
                grads.reshape(galaxy_count, chunk_samples, coeff_dim),
                jnp.pad(like_rows, ((0, 0), (0, 0), (0, coeff_dim - galaxy_count))),
            ],
            axis=0,
        )
        mine = lax.psum_scatter(flat, "expo", scatter_dimension=1, tiled=True)
        grad_pieces.append(mine[:galaxy_count])
        like_pieces.append(mine[galaxy_count, :, :galaxy_count].T)
    grad_out = jnp.concatenate(grad_pieces, axis=1)
    like_out = jnp.concatenate(like_pieces, axis=1)
    return (like_out, grad_out)


def solution(mesh):
    placed = (
        P("sky", None, None),
        P(),
        P(("expo", "sky"), None, None),
        P(("expo", "sky"), None, None),
        P(("expo", "sky"), None, None),
        P("expo", "sky", None, None),
        P(("expo", "sky"), None),
    )
    return jax.shard_map(
        per_device,
        mesh=mesh,
        in_specs=placed,
        out_specs=(P("sky", "expo"), P("sky", "expo", None)),
        check_vma=False,
    )
```

```python
import jax
import jax.numpy as jnp
from jax import lax
from jax.sharding import PartitionSpec as P

N_CHUNKS = 2
LANE = 128


def per_device(samples, basis, operators, cutouts, pixel_weights, detections, intersections):
    tiles_here, tile_cap, pixels = cutouts.shape
    coeff_dim = basis.shape[0]
    galaxy_count, sample_count, _unused = samples.shape
    sky_count = lax.axis_size("sky")
    expo_count = lax.axis_size("expo")
    send_cap = detections.shape[3]
    slot_count = sky_count * send_cap
    per_expo = sample_count // expo_count
    chunk_size = per_expo // N_CHUNKS
    chunk_samples = expo_count * chunk_size
    sent_rows = detections.reshape(sky_count, send_cap)
    positions = tiles_here * tile_cap
    block = chunk_size * coeff_dim
    like_width = slot_count // sky_count * chunk_size
    like_pad = -like_width % LANE

    arranged = samples.reshape(galaxy_count, expo_count, N_CHUNKS, chunk_size, coeff_dim)
    arranged = arranged.transpose(0, 2, 1, 3, 4).reshape(galaxy_count, N_CHUNKS, -1)
    send_index = jnp.maximum(sent_rows, 0).reshape(-1)
    live = intersections >= 0
    pick = jnp.maximum(intersections, 0).reshape(-1)
    target = jnp.where(live, intersections, slot_count).reshape(-1)
    holder = jnp.full((slot_count,), positions, jnp.int32)
    holder = holder.at[target].set(jnp.arange(positions, dtype=jnp.int32), mode="drop")

    listed_all = lax.all_gather(sent_rows, "expo", axis=0, tiled=False).reshape(-1)
    onehot = (listed_all[None, :] == jnp.arange(galaxy_count, dtype=jnp.int32)[:, None]).astype(
        jnp.float32
    )

    grad_pieces = []
    like_pieces = []
    for chunk in range(N_CHUNKS):
        sent = jnp.take(arranged[:, chunk], send_index, axis=0, mode="clip")
        sent = sent.reshape(sky_count, send_cap, chunk_samples * coeff_dim)
        incoming = lax.all_to_all(sent, "sky", split_axis=0, concat_axis=0, tiled=True)
        incoming = incoming.reshape(slot_count, chunk_samples * coeff_dim)
        picked = jnp.take(incoming, pick, axis=0, mode="clip").reshape(-1, coeff_dim)
        rendered = jnp.dot(picked, basis, preferred_element_type=jnp.float32).astype(jnp.bfloat16)
        rendered = rendered.reshape(tiles_here, tile_cap * chunk_samples, pixels)
        model = jnp.einsum("tnp,tpq->tnq", rendered, operators, preferred_element_type=jnp.float32)
        model = model.reshape(tiles_here, tile_cap, chunk_samples, pixels)
        resid = model - cutouts[:, :, None, :]
        weighted = pixel_weights[:, :, None, :] * resid
        pair_like = -0.5 / pixels * jnp.sum(weighted * resid, axis=-1)
        scaled = weighted.astype(jnp.bfloat16).reshape(tiles_here, tile_cap * chunk_samples, pixels)
        backed = jnp.einsum(
            "tnq,tpq->tnp", scaled, operators, preferred_element_type=jnp.float32
        ).astype(jnp.bfloat16)
        pair_grad = (
            -1.0
            / pixels
            * lax.dot_general(
                backed.reshape(-1, pixels),
                basis,
                (((1,), (1,)), ((), ())),
                preferred_element_type=jnp.float32,
            )
        )
        grad_rows = pair_grad.reshape(positions, expo_count, block).transpose(1, 0, 2)
        like_rows = pair_like.reshape(positions, expo_count, chunk_size).transpose(1, 0, 2)
        slot_grads = jnp.take(grad_rows, holder, axis=1, mode="fill", fill_value=0.0)
        slot_likes = jnp.take(like_rows, holder, axis=1, mode="fill", fill_value=0.0)
        send_back = jnp.concatenate(
            [
                slot_grads.reshape(expo_count, sky_count, send_cap * block),
                slot_likes.reshape(expo_count, sky_count, like_width),
                jnp.zeros((expo_count, sky_count, like_pad), jnp.float32),
            ],
            axis=2,
        ).reshape(expo_count * sky_count, -1)
        back = lax.all_to_all(
            send_back, ("expo", "sky"), split_axis=0, concat_axis=0, tiled=True
        )
        back_grads = back[:, : send_cap * block].reshape(-1, block)
        back_likes = back[:, send_cap * block : send_cap * block + like_width].reshape(
            -1, chunk_size
        )
        grads = jnp.dot(onehot, back_grads, precision=lax.Precision.HIGHEST)
        likes = jnp.dot(onehot, back_likes, precision=lax.Precision.HIGHEST)
        grad_pieces.append(grads.reshape(galaxy_count, chunk_size, coeff_dim))
        like_pieces.append(likes)
    grad_out = jnp.concatenate(grad_pieces, axis=1)
    like_out = jnp.concatenate(like_pieces, axis=1)
    return (like_out, grad_out)


def solution(mesh):
    placed = (
        P("sky", None, None),
        P(),
        P(("expo", "sky"), None, None),
        P(("expo", "sky"), None, None),
        P(("expo", "sky"), None, None),
        P("expo", "sky", None, None),
        P(("expo", "sky"), None),
    )
    return jax.shard_map(
        per_device,
        mesh=mesh,
        in_specs=placed,
        out_specs=(P("sky", "expo"), P("sky", "expo", None)),
        check_vma=False,
    )
```

```python
import jax
import jax.numpy as jnp
from jax import lax
from jax.sharding import PartitionSpec as P

N_CHUNKS = 2
LANE = 128


def per_device(samples, basis, operators, cutouts, pixel_weights, detections, intersections):
    tiles_here, tile_cap, pixels = cutouts.shape
    coeff_dim = basis.shape[0]
    galaxy_count, sample_count, _unused = samples.shape
    sky_count = lax.axis_size("sky")
    expo_count = lax.axis_size("expo")
    send_cap = detections.shape[3]
    slot_count = sky_count * send_cap
    per_expo = sample_count // expo_count
    chunk_size = per_expo // N_CHUNKS
    chunk_samples = expo_count * chunk_size
    positions = tiles_here * tile_cap
    devices = expo_count * sky_count

    listed_all = lax.all_gather(
        detections.reshape(sky_count, send_cap), "expo", axis=0, tiled=False
    )
    sent_rows = lax.dynamic_index_in_dim(listed_all, lax.axis_index("expo"), 0, keepdims=False)
    listed_flat = listed_all.reshape(-1)
    onehot = (listed_flat[None, :] == jnp.arange(galaxy_count, dtype=jnp.int32)[:, None]).astype(
        jnp.float32
    )
    onehot_k = (
        onehot[:, None, :, None]
        * jnp.eye(chunk_size, dtype=jnp.float32)[None, :, None, :]
    ).reshape(galaxy_count * chunk_size, -1)

    arranged = samples.reshape(galaxy_count, expo_count, N_CHUNKS, chunk_size, coeff_dim)
    arranged = arranged.transpose(2, 0, 1, 3, 4).reshape(N_CHUNKS, -1, coeff_dim)
    sample_ids = jnp.arange(chunk_samples, dtype=jnp.int32)
    send_index = (jnp.maximum(sent_rows, 0).reshape(-1, 1) * chunk_samples + sample_ids).reshape(-1)
    live = intersections >= 0
    pick = jnp.maximum(intersections, 0).reshape(-1)
    pick_index = (pick.reshape(-1, 1) * chunk_samples + sample_ids).reshape(-1)
    target = jnp.where(live, intersections, slot_count).reshape(-1)
    holder = jnp.full((slot_count,), positions, jnp.int32)
    holder = holder.at[target].set(jnp.arange(positions, dtype=jnp.int32), mode="drop")
    expo_ids = jnp.arange(expo_count, dtype=jnp.int32)
    k_ids = jnp.arange(chunk_size, dtype=jnp.int32)
    back_index = (
        (holder[None, :, None] * expo_count + expo_ids[:, None, None]) * chunk_size
        + k_ids[None, None, :]
    )
    back_index = jnp.where(holder[None, :, None] < positions, back_index, positions * chunk_samples)
    back_index = back_index.reshape(-1)

    grad_pieces = []
    like_rows = []
    for chunk in range(N_CHUNKS):
        sent = jnp.take(arranged[chunk], send_index, axis=0, mode="clip")
        incoming = lax.all_to_all(sent, "sky", split_axis=0, concat_axis=0, tiled=True)
        picked = jnp.take(incoming, pick_index, axis=0, mode="clip")
        rendered = jnp.dot(picked, basis, preferred_element_type=jnp.float32).astype(jnp.bfloat16)
        rendered = rendered.reshape(tiles_here, tile_cap * chunk_samples, pixels)
        model = jnp.einsum("tnp,tpq->tnq", rendered, operators, preferred_element_type=jnp.float32)
        model = model.reshape(tiles_here, tile_cap, chunk_samples, pixels)
        resid = model - cutouts[:, :, None, :]
        weighted = pixel_weights[:, :, None, :] * resid
        pair_like = -0.5 / pixels * jnp.sum(weighted * resid, axis=-1)
        scaled = weighted.astype(jnp.bfloat16).reshape(tiles_here, tile_cap * chunk_samples, pixels)
        backed = jnp.einsum(
            "tnq,tpq->tnp", scaled, operators, preferred_element_type=jnp.float32
        ).astype(jnp.bfloat16)
        pair_grad = (
            -1.0
            / pixels
            * lax.dot_general(
                backed.reshape(-1, pixels),
                basis,
                (((1,), (1,)), ((), ())),
                preferred_element_type=jnp.float32,
            )
        )
        send_back = jnp.take(pair_grad, back_index, axis=0, mode="fill", fill_value=0.0)
        back = lax.all_to_all(send_back, ("expo", "sky"), split_axis=0, concat_axis=0, tiled=True)
        grads = jnp.dot(onehot_k, back, precision=lax.Precision.HIGHEST)
        grad_pieces.append(grads.reshape(galaxy_count, chunk_size, coeff_dim))
        like_rows.append(pair_like.reshape(positions, expo_count, chunk_size))
    likes = jnp.stack(like_rows, axis=2).reshape(positions, expo_count, per_expo)
    likes = jnp.take(likes.transpose(1, 0, 2), holder, axis=1, mode="fill", fill_value=0.0)
    like_width = send_cap * per_expo
    likes = likes.reshape(devices, like_width)
    likes = jnp.pad(likes, ((0, 0), (0, -like_width % LANE)))
    back_likes = lax.all_to_all(likes, ("expo", "sky"), split_axis=0, concat_axis=0, tiled=True)
    back_likes = back_likes[:, :like_width].reshape(-1, per_expo)
    like_out = jnp.dot(onehot, back_likes, precision=lax.Precision.HIGHEST)
    grad_out = jnp.concatenate(grad_pieces, axis=1)
    return (like_out, grad_out)


def solution(mesh):
    placed = (
        P("sky", None, None),
        P(),
        P(("expo", "sky"), None, None),
        P(("expo", "sky"), None, None),
        P(("expo", "sky"), None, None),
        P("expo", "sky", None, None),
        P(("expo", "sky"), None),
    )
    return jax.shard_map(
        per_device,
        mesh=mesh,
        in_specs=placed,
        out_specs=(P("sky", "expo"), P("sky", "expo", None)),
        check_vma=False,
    )
```

```python
import jax
import jax.numpy as jnp
from jax import lax
from jax.sharding import PartitionSpec as P

N_CHUNKS = 2
LANE = 128


def select(rows, cols):
    return (rows[:, None] == cols[None, :]).astype(jnp.bfloat16)


def per_device(samples, basis, operators, cutouts, pixel_weights, detections, intersections):
    tiles_here, tile_cap, pixels = cutouts.shape
    coeff_dim = basis.shape[0]
    galaxy_count, sample_count, _unused = samples.shape
    sky_count = lax.axis_size("sky")
    expo_count = lax.axis_size("expo")
    send_cap = detections.shape[3]
    slot_count = sky_count * send_cap
    per_expo = sample_count // expo_count
    chunk_size = per_expo // N_CHUNKS
    chunk_samples = expo_count * chunk_size
    positions = tiles_here * tile_cap
    devices = expo_count * sky_count

    listed_all = lax.all_gather(
        detections.reshape(sky_count, send_cap), "expo", axis=0, tiled=False
    )
    sent_rows = lax.dynamic_index_in_dim(listed_all, lax.axis_index("expo"), 0, keepdims=False)
    listed_flat = listed_all.reshape(-1)
    onehot = (listed_flat[None, :] == jnp.arange(galaxy_count, dtype=jnp.int32)[:, None]).astype(
        jnp.float32
    )
    onehot_k = (
        onehot[:, None, :, None]
        * jnp.eye(chunk_size, dtype=jnp.float32)[None, :, None, :]
    ).reshape(galaxy_count * chunk_size, -1)

    arranged = samples.reshape(galaxy_count, expo_count, N_CHUNKS, chunk_size, coeff_dim)
    arranged = arranged.transpose(2, 0, 1, 3, 4).reshape(N_CHUNKS, -1, coeff_dim)
    m_ids = jnp.arange(chunk_samples, dtype=jnp.int32)
    send_src = jnp.where(
        sent_rows.reshape(-1, 1) >= 0, sent_rows.reshape(-1, 1) * chunk_samples + m_ids, -1
    ).reshape(-1)
    send_select = select(send_src, jnp.arange(galaxy_count * chunk_samples, dtype=jnp.int32))
    pick = jnp.maximum(intersections, 0)
    pick_src = (pick[:, None, :] * chunk_samples + m_ids[None, :, None]).reshape(-1)
    pick_select = select(pick_src, jnp.arange(slot_count * chunk_samples, dtype=jnp.int32))
    live = intersections >= 0
    target = jnp.where(live, intersections, slot_count).reshape(-1)
    holder = jnp.full((slot_count,), positions, jnp.int32)
    holder = holder.at[target].set(jnp.arange(positions, dtype=jnp.int32), mode="drop")
    k_ids = jnp.arange(chunk_size, dtype=jnp.int32)
    back_src = (k_ids[None, :] * positions + holder[:, None]).reshape(-1)
    back_src = jnp.where(jnp.repeat(holder, chunk_size) < positions, back_src, -1)
    back_select = select(back_src, jnp.arange(chunk_size * positions, dtype=jnp.int32))
    back_select = jnp.broadcast_to(
        back_select.astype(jnp.float32)[None], (expo_count,) + back_select.shape
    )

    grad_pieces = []
    like_rows = []
    for chunk in range(N_CHUNKS):
        sent = jnp.dot(
            send_select, arranged[chunk], preferred_element_type=jnp.float32
        ).astype(jnp.bfloat16)
        incoming = lax.all_to_all(sent, "sky", split_axis=0, concat_axis=0, tiled=True)
        picked = jnp.dot(pick_select, incoming, preferred_element_type=jnp.float32).astype(
            jnp.bfloat16
        )
        rendered = jnp.dot(picked, basis, preferred_element_type=jnp.float32).astype(jnp.bfloat16)
        rendered = rendered.reshape(tiles_here, chunk_samples * tile_cap, pixels)
        model = jnp.einsum("tnp,tpq->tnq", rendered, operators, preferred_element_type=jnp.float32)
        model = model.reshape(tiles_here, chunk_samples, tile_cap, pixels)
        resid = model - cutouts[:, None, :, :]
        weighted = pixel_weights[:, None, :, :] * resid
        pair_like = -0.5 / pixels * jnp.sum(weighted * resid, axis=-1)
        scaled = weighted.astype(jnp.bfloat16).reshape(tiles_here, chunk_samples * tile_cap, pixels)
        backed = jnp.einsum(
            "tnq,tpq->tnp", scaled, operators, preferred_element_type=jnp.float32
        ).astype(jnp.bfloat16)
        pair_grad = (
            -1.0
            / pixels
            * lax.dot_general(
                backed.reshape(-1, pixels),
                basis,
                (((1,), (1,)), ((), ())),
                preferred_element_type=jnp.float32,
            )
        )
        grad_src = pair_grad.reshape(tiles_here, expo_count, chunk_size, tile_cap, coeff_dim)
        grad_src = grad_src.transpose(1, 2, 0, 3, 4).reshape(expo_count, -1, coeff_dim)
        send_back = lax.dot_general(
            back_select,
            grad_src,
            (((2,), (1,)), ((0,), (0,))),
            precision=lax.Precision.HIGHEST,
            preferred_element_type=jnp.float32,
        ).reshape(-1, coeff_dim)
        back = lax.all_to_all(send_back, ("expo", "sky"), split_axis=0, concat_axis=0, tiled=True)
        grads = jnp.dot(onehot_k, back, precision=lax.Precision.HIGHEST)
        grad_pieces.append(grads.reshape(galaxy_count, chunk_size, coeff_dim))
        like_rows.append(
            pair_like.reshape(tiles_here, expo_count, chunk_size, tile_cap).transpose(1, 2, 0, 3)
        )
    likes = jnp.stack(like_rows, axis=1).reshape(expo_count, per_expo, positions)
    likes = jnp.take(likes, holder, axis=2, mode="fill", fill_value=0.0).transpose(0, 2, 1)
    like_width = send_cap * per_expo
    likes = likes.reshape(devices, like_width)
    likes = jnp.pad(likes, ((0, 0), (0, -like_width % LANE)))
    back_likes = lax.all_to_all(likes, ("expo", "sky"), split_axis=0, concat_axis=0, tiled=True)
    back_likes = back_likes[:, :like_width].reshape(-1, per_expo)
    like_out = jnp.dot(onehot, back_likes, precision=lax.Precision.HIGHEST)
    grad_out = jnp.concatenate(grad_pieces, axis=1)
    return (like_out, grad_out)


def solution(mesh):
    placed = (
        P("sky", None, None),
        P(),
        P(("expo", "sky"), None, None),
        P(("expo", "sky"), None, None),
        P(("expo", "sky"), None, None),
        P("expo", "sky", None, None),
        P(("expo", "sky"), None),
    )
    return jax.shard_map(
        per_device,
        mesh=mesh,
        in_specs=placed,
        out_specs=(P("sky", "expo"), P("sky", "expo", None)),
        check_vma=False,
    )
```

```python
import jax
import jax.numpy as jnp
from jax import lax
from jax.sharding import PartitionSpec as P

N_CHUNKS = 4
LANE = 128


def select(rows, cols):
    return (rows[:, None] == cols[None, :]).astype(jnp.bfloat16)


def per_device(samples, basis, operators, cutouts, pixel_weights, detections, intersections):
    tiles_here, tile_cap, pixels = cutouts.shape
    coeff_dim = basis.shape[0]
    galaxy_count, sample_count, _unused = samples.shape
    sky_count = lax.axis_size("sky")
    expo_count = lax.axis_size("expo")
    send_cap = detections.shape[3]
    slot_count = sky_count * send_cap
    per_expo = sample_count // expo_count
    chunk_size = per_expo // N_CHUNKS
    chunk_samples = expo_count * chunk_size
    positions = tiles_here * tile_cap
    devices = expo_count * sky_count

    listed_all = lax.all_gather(
        detections.reshape(sky_count, send_cap), "expo", axis=0, tiled=False
    )
    sent_rows = lax.dynamic_index_in_dim(listed_all, lax.axis_index("expo"), 0, keepdims=False)
    listed_flat = listed_all.reshape(-1)
    onehot = (listed_flat[None, :] == jnp.arange(galaxy_count, dtype=jnp.int32)[:, None]).astype(
        jnp.float32
    )
    onehot_k = (
        onehot[:, None, :, None]
        * jnp.eye(chunk_size, dtype=jnp.float32)[None, :, None, :]
    ).reshape(galaxy_count * chunk_size, -1)

    arranged = samples.reshape(galaxy_count, expo_count, N_CHUNKS, chunk_size, coeff_dim)
    arranged = arranged.transpose(2, 0, 1, 3, 4).reshape(N_CHUNKS, -1, coeff_dim)
    m_ids = jnp.arange(chunk_samples, dtype=jnp.int32)
    send_src = jnp.where(
        sent_rows.reshape(-1, 1) >= 0, sent_rows.reshape(-1, 1) * chunk_samples + m_ids, -1
    ).reshape(-1)
    send_select = select(send_src, jnp.arange(galaxy_count * chunk_samples, dtype=jnp.int32))
    pick = jnp.maximum(intersections, 0)
    pick_src = (pick[:, None, :] * chunk_samples + m_ids[None, :, None]).reshape(-1)
    pick_select = select(pick_src, jnp.arange(slot_count * chunk_samples, dtype=jnp.int32))
    live = intersections >= 0
    target = jnp.where(live, intersections, slot_count).reshape(-1)
    holder = jnp.full((slot_count,), positions, jnp.int32)
    holder = holder.at[target].set(jnp.arange(positions, dtype=jnp.int32), mode="drop")
    k_ids = jnp.arange(chunk_size, dtype=jnp.int32)
    back_src = (k_ids[None, :] * positions + holder[:, None]).reshape(-1)
    back_src = jnp.where(jnp.repeat(holder, chunk_size) < positions, back_src, -1)
    back_select = select(back_src, jnp.arange(chunk_size * positions, dtype=jnp.int32))
    back_select = jnp.broadcast_to(
        back_select.astype(jnp.float32)[None], (expo_count,) + back_select.shape
    )

    grad_pieces = []
    like_rows = []
    for chunk in range(N_CHUNKS):
        sent = jnp.dot(
            send_select, arranged[chunk], preferred_element_type=jnp.float32
        ).astype(jnp.bfloat16)
        incoming = lax.all_to_all(sent, "sky", split_axis=0, concat_axis=0, tiled=True)
        picked = jnp.dot(pick_select, incoming, preferred_element_type=jnp.float32).astype(
            jnp.bfloat16
        )
        rendered = jnp.dot(picked, basis, preferred_element_type=jnp.float32).astype(jnp.bfloat16)
        rendered = rendered.reshape(tiles_here, chunk_samples * tile_cap, pixels)
        model = jnp.einsum("tnp,tpq->tnq", rendered, operators, preferred_element_type=jnp.float32)
        model = model.reshape(tiles_here, chunk_samples, tile_cap, pixels)
        resid = model - cutouts[:, None, :, :]
        weighted = pixel_weights[:, None, :, :] * resid
        pair_like = -0.5 / pixels * jnp.sum(weighted * resid, axis=-1)
        scaled = weighted.astype(jnp.bfloat16).reshape(tiles_here, chunk_samples * tile_cap, pixels)
        backed = jnp.einsum(
            "tnq,tpq->tnp", scaled, operators, preferred_element_type=jnp.float32
        ).astype(jnp.bfloat16)
        pair_grad = (
            -1.0
            / pixels
            * lax.dot_general(
                backed.reshape(-1, pixels),
                basis,
                (((1,), (1,)), ((), ())),
                preferred_element_type=jnp.float32,
            )
        )
        grad_src = pair_grad.reshape(tiles_here, expo_count, chunk_size, tile_cap, coeff_dim)
        grad_src = grad_src.transpose(1, 2, 0, 3, 4).reshape(expo_count, -1, coeff_dim)
        send_back = lax.dot_general(
            back_select,
            grad_src,
            (((2,), (1,)), ((0,), (0,))),
            precision=lax.Precision.HIGHEST,
            preferred_element_type=jnp.float32,
        ).reshape(-1, coeff_dim)
        back = lax.all_to_all(send_back, ("expo", "sky"), split_axis=0, concat_axis=0, tiled=True)
        grads = jnp.dot(onehot_k, back, precision=lax.Precision.HIGHEST)
        grad_pieces.append(grads.reshape(galaxy_count, chunk_size, coeff_dim))
        like_rows.append(
            pair_like.reshape(tiles_here, expo_count, chunk_size, tile_cap).transpose(1, 2, 0, 3)
        )
    likes = jnp.stack(like_rows, axis=1).reshape(expo_count, per_expo, positions)
    likes = jnp.take(likes, holder, axis=2, mode="fill", fill_value=0.0).transpose(0, 2, 1)
    like_width = send_cap * per_expo
    likes = likes.reshape(devices, like_width)
    likes = jnp.pad(likes, ((0, 0), (0, -like_width % LANE)))
    back_likes = lax.all_to_all(likes, ("expo", "sky"), split_axis=0, concat_axis=0, tiled=True)
    back_likes = back_likes[:, :like_width].reshape(-1, per_expo)
    like_out = jnp.dot(onehot, back_likes, precision=lax.Precision.HIGHEST)
    grad_out = jnp.concatenate(grad_pieces, axis=1)
    return (like_out, grad_out)


def solution(mesh):
    placed = (
        P("sky", None, None),
        P(),
        P(("expo", "sky"), None, None),
        P(("expo", "sky"), None, None),
        P(("expo", "sky"), None, None),
        P("expo", "sky", None, None),
        P(("expo", "sky"), None),
    )
    return jax.shard_map(
        per_device,
        mesh=mesh,
        in_specs=placed,
        out_specs=(P("sky", "expo"), P("sky", "expo", None)),
        check_vma=False,
    )
```

```python
import jax
import jax.numpy as jnp
from jax import lax
from jax.sharding import PartitionSpec as P

N_CHUNKS = 2
LANE = 128


def select(rows, cols):
    return (rows[:, None] == cols[None, :]).astype(jnp.bfloat16)


def per_device(samples, basis, operators, cutouts, pixel_weights, detections, intersections):
    tiles_here, tile_cap, pixels = cutouts.shape
    coeff_dim = basis.shape[0]
    galaxy_count, sample_count, _unused = samples.shape
    sky_count = lax.axis_size("sky")
    expo_count = lax.axis_size("expo")
    send_cap = detections.shape[3]
    slot_count = sky_count * send_cap
    per_expo = sample_count // expo_count
    chunk_size = per_expo // N_CHUNKS
    chunk_samples = expo_count * chunk_size
    positions = tiles_here * tile_cap
    devices = expo_count * sky_count

    listed_all = lax.all_gather(
        detections.reshape(sky_count, send_cap), "expo", axis=0, tiled=False
    )
    sent_rows = lax.dynamic_index_in_dim(listed_all, lax.axis_index("expo"), 0, keepdims=False)
    listed_flat = listed_all.reshape(-1)
    onehot = (listed_flat[None, :] == jnp.arange(galaxy_count, dtype=jnp.int32)[:, None]).astype(
        jnp.float32
    )
    onehot_k = (
        onehot[:, None, :, None]
        * jnp.eye(chunk_size, dtype=jnp.float32)[None, :, None, :]
    ).reshape(galaxy_count * chunk_size, -1)

    arranged = samples.reshape(galaxy_count, expo_count, N_CHUNKS, chunk_size, coeff_dim)
    arranged = arranged.transpose(2, 0, 1, 3, 4).reshape(N_CHUNKS, -1, coeff_dim)
    m_ids = jnp.arange(chunk_samples, dtype=jnp.int32)
    send_src = jnp.where(
        sent_rows.reshape(-1, 1) >= 0, sent_rows.reshape(-1, 1) * chunk_samples + m_ids, -1
    ).reshape(-1)
    send_select = select(send_src, jnp.arange(galaxy_count * chunk_samples, dtype=jnp.int32))
    pick = jnp.maximum(intersections, 0)
    pick_src = (pick[:, None, :] * chunk_samples + m_ids[None, :, None]).reshape(-1)
    pick_select = select(pick_src, jnp.arange(slot_count * chunk_samples, dtype=jnp.int32))
    live = intersections >= 0
    target = jnp.where(live, intersections, slot_count).reshape(-1)
    holder = jnp.full((slot_count,), positions, jnp.int32)
    holder = holder.at[target].set(jnp.arange(positions, dtype=jnp.int32), mode="drop")
    k_ids = jnp.arange(chunk_size, dtype=jnp.int32)
    back_src = (k_ids[None, :] * positions + holder[:, None]).reshape(-1)
    back_src = jnp.where(jnp.repeat(holder, chunk_size) < positions, back_src, -1)
    back_select = select(back_src, jnp.arange(chunk_size * positions, dtype=jnp.int32))
    back_select = jnp.broadcast_to(
        back_select.astype(jnp.float32)[None], (expo_count,) + back_select.shape
    )

    def send_home(send_back):
        back = lax.all_to_all(send_back, ("expo", "sky"), split_axis=0, concat_axis=0, tiled=True)
        grads = jnp.dot(onehot_k, back, precision=lax.Precision.HIGHEST)
        return grads.reshape(galaxy_count, chunk_size, coeff_dim)

    grad_pieces = []
    like_rows = []
    pending = None
    for chunk in range(N_CHUNKS):
        sent = jnp.dot(
            send_select, arranged[chunk], preferred_element_type=jnp.float32
        ).astype(jnp.bfloat16)
        incoming = lax.all_to_all(sent, "sky", split_axis=0, concat_axis=0, tiled=True)
        if pending is not None:
            pending, incoming = lax.optimization_barrier((pending, incoming))
            grad_pieces.append(send_home(pending))
        picked = jnp.dot(pick_select, incoming, preferred_element_type=jnp.float32).astype(
            jnp.bfloat16
        )
        rendered = jnp.dot(picked, basis, preferred_element_type=jnp.float32).astype(jnp.bfloat16)
        rendered = rendered.reshape(tiles_here, chunk_samples * tile_cap, pixels)
        model = jnp.einsum("tnp,tpq->tnq", rendered, operators, preferred_element_type=jnp.float32)
        model = model.reshape(tiles_here, chunk_samples, tile_cap, pixels)
        resid = model - cutouts[:, None, :, :]
        weighted = pixel_weights[:, None, :, :] * resid
        pair_like = -0.5 / pixels * jnp.sum(weighted * resid, axis=-1)
        scaled = weighted.astype(jnp.bfloat16).reshape(tiles_here, chunk_samples * tile_cap, pixels)
        backed = jnp.einsum(
            "tnq,tpq->tnp", scaled, operators, preferred_element_type=jnp.float32
        ).astype(jnp.bfloat16)
        pair_grad = (
            -1.0
            / pixels
            * lax.dot_general(
                backed.reshape(-1, pixels),
                basis,
                (((1,), (1,)), ((), ())),
                preferred_element_type=jnp.float32,
            )
        )
        grad_src = pair_grad.reshape(tiles_here, expo_count, chunk_size, tile_cap, coeff_dim)
        grad_src = grad_src.transpose(1, 2, 0, 3, 4).reshape(expo_count, -1, coeff_dim)
        send_back = lax.dot_general(
            back_select,
            grad_src,
            (((2,), (1,)), ((0,), (0,))),
            precision=lax.Precision.HIGHEST,
            preferred_element_type=jnp.float32,
        ).reshape(-1, coeff_dim)
        pending = send_back
        like_rows.append(
            pair_like.reshape(tiles_here, expo_count, chunk_size, tile_cap).transpose(1, 2, 0, 3)
        )
    grad_pieces.append(send_home(pending))
    likes = jnp.stack(like_rows, axis=1).reshape(expo_count, per_expo, positions)
    likes = jnp.take(likes, holder, axis=2, mode="fill", fill_value=0.0).transpose(0, 2, 1)
    like_width = send_cap * per_expo
    likes = likes.reshape(devices, like_width)
    likes = jnp.pad(likes, ((0, 0), (0, -like_width % LANE)))
    back_likes = lax.all_to_all(likes, ("expo", "sky"), split_axis=0, concat_axis=0, tiled=True)
    back_likes = back_likes[:, :like_width].reshape(-1, per_expo)
    like_out = jnp.dot(onehot, back_likes, precision=lax.Precision.HIGHEST)
    grad_out = jnp.concatenate(grad_pieces, axis=1)
    return (like_out, grad_out)


def solution(mesh):
    placed = (
        P("sky", None, None),
        P(),
        P(("expo", "sky"), None, None),
        P(("expo", "sky"), None, None),
        P(("expo", "sky"), None, None),
        P("expo", "sky", None, None),
        P(("expo", "sky"), None),
    )
    return jax.shard_map(
        per_device,
        mesh=mesh,
        in_specs=placed,
        out_specs=(P("sky", "expo"), P("sky", "expo", None)),
        check_vma=False,
    )
```

```python
import jax
import jax.numpy as jnp
from jax import lax
from jax.sharding import PartitionSpec as P

N_CHUNKS = 2
LANE = 128


def select(rows, cols):
    return (rows[:, None] == cols[None, :]).astype(jnp.bfloat16)


def per_device(samples, basis, operators, cutouts, pixel_weights, detections, intersections):
    tiles_here, tile_cap, pixels = cutouts.shape
    coeff_dim = basis.shape[0]
    galaxy_count, sample_count, _unused = samples.shape
    sky_count = lax.axis_size("sky")
    expo_count = lax.axis_size("expo")
    send_cap = detections.shape[3]
    slot_count = sky_count * send_cap
    per_expo = sample_count // expo_count
    chunk_size = per_expo // N_CHUNKS
    chunk_samples = expo_count * chunk_size
    positions = tiles_here * tile_cap
    devices = expo_count * sky_count

    sent_rows = detections.reshape(sky_count, send_cap)
    own_row = jnp.arange(expo_count, dtype=jnp.int32) == lax.axis_index("expo")
    spread = jnp.where(own_row[:, None, None], sent_rows[None].astype(jnp.float32), 0.0)
    listed_all = lax.psum(spread, "expo").astype(jnp.int32)
    listed_flat = listed_all.reshape(-1)
    onehot = (listed_flat[None, :] == jnp.arange(galaxy_count, dtype=jnp.int32)[:, None]).astype(
        jnp.float32
    )
    onehot_k = (
        onehot[:, None, :, None]
        * jnp.eye(chunk_size, dtype=jnp.float32)[None, :, None, :]
    ).reshape(galaxy_count * chunk_size, -1)

    arranged = samples.reshape(galaxy_count, expo_count, N_CHUNKS, chunk_size, coeff_dim)
    arranged = arranged.transpose(2, 0, 1, 3, 4).reshape(N_CHUNKS, -1, coeff_dim)
    m_ids = jnp.arange(chunk_samples, dtype=jnp.int32)
    send_src = jnp.where(
        sent_rows.reshape(-1, 1) >= 0, sent_rows.reshape(-1, 1) * chunk_samples + m_ids, -1
    ).reshape(-1)
    send_select = select(send_src, jnp.arange(galaxy_count * chunk_samples, dtype=jnp.int32))
    pick = jnp.maximum(intersections, 0)
    pick_src = (pick[:, None, :] * chunk_samples + m_ids[None, :, None]).reshape(-1)
    pick_select = select(pick_src, jnp.arange(slot_count * chunk_samples, dtype=jnp.int32))
    live = intersections >= 0
    target = jnp.where(live, intersections, slot_count).reshape(-1)
    holder = jnp.full((slot_count,), positions, jnp.int32)
    holder = holder.at[target].set(jnp.arange(positions, dtype=jnp.int32), mode="drop")
    k_ids = jnp.arange(chunk_size, dtype=jnp.int32)
    back_src = (k_ids[None, :] * positions + holder[:, None]).reshape(-1)
    back_src = jnp.where(jnp.repeat(holder, chunk_size) < positions, back_src, -1)
    back_select = select(back_src, jnp.arange(chunk_size * positions, dtype=jnp.int32))
    back_select = jnp.broadcast_to(
        back_select.astype(jnp.float32)[None], (expo_count,) + back_select.shape
    )

    grad_pieces = []
    like_rows = []
    for chunk in range(N_CHUNKS):
        sent = jnp.dot(
            send_select, arranged[chunk], preferred_element_type=jnp.float32
        ).astype(jnp.bfloat16)
        incoming = lax.all_to_all(sent, "sky", split_axis=0, concat_axis=0, tiled=True)
        picked = jnp.dot(pick_select, incoming, preferred_element_type=jnp.float32).astype(
            jnp.bfloat16
        )
        rendered = jnp.dot(picked, basis, preferred_element_type=jnp.float32).astype(jnp.bfloat16)
        rendered = rendered.reshape(tiles_here, chunk_samples * tile_cap, pixels)
        model = jnp.einsum("tnp,tpq->tnq", rendered, operators, preferred_element_type=jnp.float32)
        model = model.reshape(tiles_here, chunk_samples, tile_cap, pixels)
        resid = model - cutouts[:, None, :, :]
        weighted = pixel_weights[:, None, :, :] * resid
        pair_like = -0.5 / pixels * jnp.sum(weighted * resid, axis=-1)
        scaled = weighted.astype(jnp.bfloat16).reshape(tiles_here, chunk_samples * tile_cap, pixels)
        backed = jnp.einsum(
            "tnq,tpq->tnp", scaled, operators, preferred_element_type=jnp.float32
        ).astype(jnp.bfloat16)
        pair_grad = (
            -1.0
            / pixels
            * lax.dot_general(
                backed.reshape(-1, pixels),
                basis,
                (((1,), (1,)), ((), ())),
                preferred_element_type=jnp.float32,
            )
        )
        grad_src = pair_grad.reshape(tiles_here, expo_count, chunk_size, tile_cap, coeff_dim)
        grad_src = grad_src.transpose(1, 2, 0, 3, 4).reshape(expo_count, -1, coeff_dim)
        send_back = lax.dot_general(
            back_select,
            grad_src,
            (((2,), (1,)), ((0,), (0,))),
            precision=lax.Precision.HIGHEST,
            preferred_element_type=jnp.float32,
        ).reshape(-1, coeff_dim)
        back = lax.all_to_all(send_back, ("expo", "sky"), split_axis=0, concat_axis=0, tiled=True)
        grads = jnp.dot(onehot_k, back, precision=lax.Precision.HIGHEST)
        grad_pieces.append(grads.reshape(galaxy_count, chunk_size, coeff_dim))
        like_rows.append(
            pair_like.reshape(tiles_here, expo_count, chunk_size, tile_cap).transpose(1, 2, 0, 3)
        )
    likes = jnp.stack(like_rows, axis=1).reshape(expo_count, per_expo, positions)
    likes = jnp.take(likes, holder, axis=2, mode="fill", fill_value=0.0).transpose(0, 2, 1)
    like_width = send_cap * per_expo
    likes = likes.reshape(devices, like_width)
    likes = jnp.pad(likes, ((0, 0), (0, -like_width % LANE)))
    back_likes = lax.all_to_all(likes, ("expo", "sky"), split_axis=0, concat_axis=0, tiled=True)
    back_likes = back_likes[:, :like_width].reshape(-1, per_expo)
    like_out = jnp.dot(onehot, back_likes, precision=lax.Precision.HIGHEST)
    grad_out = jnp.concatenate(grad_pieces, axis=1)
    return (like_out, grad_out)


def solution(mesh):
    placed = (
        P("sky", None, None),
        P(),
        P(("expo", "sky"), None, None),
        P(("expo", "sky"), None, None),
        P(("expo", "sky"), None, None),
        P("expo", "sky", None, None),
        P(("expo", "sky"), None),
    )
    return jax.shard_map(
        per_device,
        mesh=mesh,
        in_specs=placed,
        out_specs=(P("sky", "expo"), P("sky", "expo", None)),
        check_vma=False,
    )
```

```python
import jax
import jax.numpy as jnp
from jax import lax
from jax.sharding import PartitionSpec as P

N_CHUNKS = 2
LANE = 128


def select(rows, cols):
    return (rows[:, None] == cols[None, :]).astype(jnp.bfloat16)


def per_device(samples, basis, operators, cutouts, pixel_weights, detections, intersections):
    tiles_here, tile_cap, pixels = cutouts.shape
    coeff_dim = basis.shape[0]
    galaxy_count, sample_count, _unused = samples.shape
    sky_count = lax.axis_size("sky")
    expo_count = lax.axis_size("expo")
    send_cap = detections.shape[3]
    slot_count = sky_count * send_cap
    per_expo = sample_count // expo_count
    chunk_size = per_expo // N_CHUNKS
    chunk_samples = expo_count * chunk_size
    positions = tiles_here * tile_cap
    devices = expo_count * sky_count

    sent_rows = detections.reshape(sky_count, send_cap)
    own_row = jnp.arange(expo_count, dtype=jnp.int32) == lax.axis_index("expo")
    spread = jnp.where(own_row[:, None, None], sent_rows[None].astype(jnp.float32), 0.0)
    listed_all = lax.psum(spread, "expo").astype(jnp.int32)

    arranged = samples.reshape(galaxy_count, expo_count, N_CHUNKS, chunk_size, coeff_dim)
    arranged = arranged.transpose(2, 0, 1, 3, 4).reshape(N_CHUNKS, -1, coeff_dim)
    m_ids = jnp.arange(chunk_samples, dtype=jnp.int32)
    send_src = jnp.where(
        sent_rows.reshape(-1, 1) >= 0, sent_rows.reshape(-1, 1) * chunk_samples + m_ids, -1
    ).reshape(-1)
    send_select = select(send_src, jnp.arange(galaxy_count * chunk_samples, dtype=jnp.int32))
    pick = jnp.maximum(intersections, 0)
    pick_src = (pick[:, None, :] * chunk_samples + m_ids[None, :, None]).reshape(-1)
    pick_select = select(pick_src, jnp.arange(slot_count * chunk_samples, dtype=jnp.int32))
    live = intersections >= 0
    target = jnp.where(live, intersections, slot_count).reshape(-1)
    holder = jnp.full((slot_count,), positions, jnp.int32)
    holder = holder.at[target].set(jnp.arange(positions, dtype=jnp.int32), mode="drop")
    k_ids = jnp.arange(chunk_size, dtype=jnp.int32)
    back_src = (k_ids[None, :] * positions + holder[:, None]).reshape(-1)
    back_src = jnp.where(jnp.repeat(holder, chunk_size) < positions, back_src, -1)
    back_select = select(back_src, jnp.arange(chunk_size * positions, dtype=jnp.int32))
    back_select = jnp.broadcast_to(
        back_select.astype(jnp.float32)[None], (expo_count,) + back_select.shape
    )

    def galaxy_selection(listed_all):
        listed_flat = listed_all.reshape(-1)
        onehot = (listed_flat[None, :] == jnp.arange(galaxy_count, dtype=jnp.int32)[:, None])
        onehot = onehot.astype(jnp.float32)
        onehot_k = (
            onehot[:, None, :, None]
            * jnp.eye(chunk_size, dtype=jnp.float32)[None, :, None, :]
        ).reshape(galaxy_count * chunk_size, -1)
        return onehot, onehot_k

    grad_pieces = []
    backs = []
    like_rows = []
    for chunk in range(N_CHUNKS):
        source = arranged[chunk]
        if chunk == 1:
            listed_all, source = lax.optimization_barrier((listed_all, source))
        sent = jnp.dot(send_select, source, preferred_element_type=jnp.float32).astype(
            jnp.bfloat16
        )
        incoming = lax.all_to_all(sent, "sky", split_axis=0, concat_axis=0, tiled=True)
        picked = jnp.dot(pick_select, incoming, preferred_element_type=jnp.float32).astype(
            jnp.bfloat16
        )
        rendered = jnp.dot(picked, basis, preferred_element_type=jnp.float32).astype(jnp.bfloat16)
        rendered = rendered.reshape(tiles_here, chunk_samples * tile_cap, pixels)
        model = jnp.einsum("tnp,tpq->tnq", rendered, operators, preferred_element_type=jnp.float32)
        model = model.reshape(tiles_here, chunk_samples, tile_cap, pixels)
        resid = model - cutouts[:, None, :, :]
        weighted = pixel_weights[:, None, :, :] * resid
        pair_like = -0.5 / pixels * jnp.sum(weighted * resid, axis=-1)
        scaled = weighted.astype(jnp.bfloat16).reshape(tiles_here, chunk_samples * tile_cap, pixels)
        backed = jnp.einsum(
            "tnq,tpq->tnp", scaled, operators, preferred_element_type=jnp.float32
        ).astype(jnp.bfloat16)
        pair_grad = (
            -1.0
            / pixels
            * lax.dot_general(
                backed.reshape(-1, pixels),
                basis,
                (((1,), (1,)), ((), ())),
                preferred_element_type=jnp.float32,
            )
        )
        grad_src = pair_grad.reshape(tiles_here, expo_count, chunk_size, tile_cap, coeff_dim)
        grad_src = grad_src.transpose(1, 2, 0, 3, 4).reshape(expo_count, -1, coeff_dim)
        send_back = lax.dot_general(
            back_select,
            grad_src,
            (((2,), (1,)), ((0,), (0,))),
            precision=lax.Precision.HIGHEST,
            preferred_element_type=jnp.float32,
        ).reshape(-1, coeff_dim)
        backs.append(
            lax.all_to_all(send_back, ("expo", "sky"), split_axis=0, concat_axis=0, tiled=True)
        )
        like_rows.append(
            pair_like.reshape(tiles_here, expo_count, chunk_size, tile_cap).transpose(1, 2, 0, 3)
        )
    onehot, onehot_k = galaxy_selection(listed_all)
    for back in backs:
        grads = jnp.dot(onehot_k, back, precision=lax.Precision.HIGHEST)
        grad_pieces.append(grads.reshape(galaxy_count, chunk_size, coeff_dim))
    likes = jnp.stack(like_rows, axis=1).reshape(expo_count, per_expo, positions)
    likes = jnp.take(likes, holder, axis=2, mode="fill", fill_value=0.0).transpose(0, 2, 1)
    like_width = send_cap * per_expo
    likes = likes.reshape(devices, like_width)
    likes = jnp.pad(likes, ((0, 0), (0, -like_width % LANE)))
    back_likes = lax.all_to_all(likes, ("expo", "sky"), split_axis=0, concat_axis=0, tiled=True)
    back_likes = back_likes[:, :like_width].reshape(-1, per_expo)
    like_out = jnp.dot(onehot, back_likes, precision=lax.Precision.HIGHEST)
    grad_out = jnp.concatenate(grad_pieces, axis=1)
    return (like_out, grad_out)


def solution(mesh):
    placed = (
        P("sky", None, None),
        P(),
        P(("expo", "sky"), None, None),
        P(("expo", "sky"), None, None),
        P(("expo", "sky"), None, None),
        P("expo", "sky", None, None),
        P(("expo", "sky"), None),
    )
    return jax.shard_map(
        per_device,
        mesh=mesh,
        in_specs=placed,
        out_specs=(P("sky", "expo"), P("sky", "expo", None)),
        check_vma=False,
    )
```

```python
import jax
import jax.numpy as jnp
from jax import lax
from jax.sharding import PartitionSpec as P

N_CHUNKS = 2
LANE = 128


def select(rows, cols):
    return (rows[:, None] == cols[None, :]).astype(jnp.bfloat16)


def per_device(samples, basis, operators, cutouts, pixel_weights, detections, intersections):
    tiles_here, tile_cap, pixels = cutouts.shape
    coeff_dim = basis.shape[0]
    galaxy_count, sample_count, _unused = samples.shape
    sky_count = lax.axis_size("sky")
    expo_count = lax.axis_size("expo")
    send_cap = detections.shape[3]
    slot_count = sky_count * send_cap
    per_expo = sample_count // expo_count
    chunk_size = per_expo // N_CHUNKS
    chunk_samples = expo_count * chunk_size
    positions = tiles_here * tile_cap
    devices = expo_count * sky_count

    listed_all = lax.all_gather(
        detections.reshape(sky_count, send_cap), "expo", axis=0, tiled=False
    )
    sent_rows = lax.dynamic_index_in_dim(listed_all, lax.axis_index("expo"), 0, keepdims=False)
    listed_flat = listed_all.reshape(-1)
    onehot = (listed_flat[None, :] == jnp.arange(galaxy_count, dtype=jnp.int32)[:, None]).astype(
        jnp.float32
    )
    onehot_k = (
        onehot[:, None, :, None]
        * jnp.eye(chunk_size, dtype=jnp.float32)[None, :, None, :]
    ).reshape(galaxy_count * chunk_size, -1)

    arranged = samples.reshape(galaxy_count, expo_count, N_CHUNKS, chunk_size, coeff_dim)
    arranged = arranged.transpose(2, 0, 1, 3, 4).reshape(N_CHUNKS, -1, coeff_dim)
    m_ids = jnp.arange(chunk_samples, dtype=jnp.int32)
    send_src = jnp.where(
        sent_rows.reshape(-1, 1) >= 0, sent_rows.reshape(-1, 1) * chunk_samples + m_ids, -1
    ).reshape(-1)
    send_select = select(send_src, jnp.arange(galaxy_count * chunk_samples, dtype=jnp.int32))
    pick = jnp.maximum(intersections, 0).reshape(-1)
    pick_select = select(pick, jnp.arange(slot_count, dtype=jnp.int32))
    pick_select = jnp.broadcast_to(pick_select[None], (chunk_samples,) + pick_select.shape)
    live = intersections >= 0
    target = jnp.where(live, intersections, slot_count).reshape(-1)
    holder = jnp.full((slot_count,), positions, jnp.int32)
    holder = holder.at[target].set(jnp.arange(positions, dtype=jnp.int32), mode="drop")
    k_ids = jnp.arange(chunk_size, dtype=jnp.int32)
    back_src = (k_ids[None, :] * positions + holder[:, None]).reshape(-1)
    back_src = jnp.where(jnp.repeat(holder, chunk_size) < positions, back_src, -1)
    back_select = select(back_src, jnp.arange(chunk_size * positions, dtype=jnp.int32))
    back_select = jnp.broadcast_to(
        back_select.astype(jnp.float32)[None], (expo_count,) + back_select.shape
    )

    grad_pieces = []
    like_rows = []
    for chunk in range(N_CHUNKS):
        sent = jnp.dot(
            send_select, arranged[chunk], preferred_element_type=jnp.float32
        ).astype(jnp.bfloat16)
        incoming = lax.all_to_all(sent, "sky", split_axis=0, concat_axis=0, tiled=True)
        by_sample = incoming.reshape(slot_count, chunk_samples, coeff_dim).transpose(1, 0, 2)
        picked = lax.dot_general(
            pick_select,
            by_sample,
            (((2,), (1,)), ((0,), (0,))),
            preferred_element_type=jnp.float32,
        ).astype(jnp.bfloat16)
        picked = picked.reshape(chunk_samples, tiles_here, tile_cap, coeff_dim)
        picked = picked.transpose(1, 0, 2, 3).reshape(-1, coeff_dim)
        rendered = jnp.dot(picked, basis, preferred_element_type=jnp.float32).astype(jnp.bfloat16)
        rendered = rendered.reshape(tiles_here, chunk_samples * tile_cap, pixels)
        model = jnp.einsum("tnp,tpq->tnq", rendered, operators, preferred_element_type=jnp.float32)
        model = model.reshape(tiles_here, chunk_samples, tile_cap, pixels)
        resid = model - cutouts[:, None, :, :]
        weighted = pixel_weights[:, None, :, :] * resid
        pair_like = -0.5 / pixels * jnp.sum(weighted * resid, axis=-1)
        scaled = weighted.astype(jnp.bfloat16).reshape(tiles_here, chunk_samples * tile_cap, pixels)
        backed = jnp.einsum(
            "tnq,tpq->tnp", scaled, operators, preferred_element_type=jnp.float32
        ).astype(jnp.bfloat16)
        pair_grad = (
            -1.0
            / pixels
            * lax.dot_general(
                backed.reshape(-1, pixels),
                basis,
                (((1,), (1,)), ((), ())),
                preferred_element_type=jnp.float32,
            )
        )
        grad_src = pair_grad.reshape(tiles_here, expo_count, chunk_size, tile_cap, coeff_dim)
        grad_src = grad_src.transpose(1, 2, 0, 3, 4).reshape(expo_count, -1, coeff_dim)
        send_back = lax.dot_general(
            back_select,
            grad_src,
            (((2,), (1,)), ((0,), (0,))),
            precision=lax.Precision.HIGHEST,
            preferred_element_type=jnp.float32,
        ).reshape(-1, coeff_dim)
        back = lax.all_to_all(send_back, ("expo", "sky"), split_axis=0, concat_axis=0, tiled=True)
        grads = jnp.dot(onehot_k, back, precision=lax.Precision.HIGHEST)
        grad_pieces.append(grads.reshape(galaxy_count, chunk_size, coeff_dim))
        like_rows.append(
            pair_like.reshape(tiles_here, expo_count, chunk_size, tile_cap).transpose(1, 2, 0, 3)
        )
    likes = jnp.stack(like_rows, axis=1).reshape(expo_count, per_expo, positions)
    likes = jnp.take(likes, holder, axis=2, mode="fill", fill_value=0.0).transpose(0, 2, 1)
    like_width = send_cap * per_expo
    likes = likes.reshape(devices, like_width)
    likes = jnp.pad(likes, ((0, 0), (0, -like_width % LANE)))
    back_likes = lax.all_to_all(likes, ("expo", "sky"), split_axis=0, concat_axis=0, tiled=True)
    back_likes = back_likes[:, :like_width].reshape(-1, per_expo)
    like_out = jnp.dot(onehot, back_likes, precision=lax.Precision.HIGHEST)
    grad_out = jnp.concatenate(grad_pieces, axis=1)
    return (like_out, grad_out)


def solution(mesh):
    placed = (
        P("sky", None, None),
        P(),
        P(("expo", "sky"), None, None),
        P(("expo", "sky"), None, None),
        P(("expo", "sky"), None, None),
        P("expo", "sky", None, None),
        P(("expo", "sky"), None),
    )
    return jax.shard_map(
        per_device,
        mesh=mesh,
        in_specs=placed,
        out_specs=(P("sky", "expo"), P("sky", "expo", None)),
        check_vma=False,
    )
```

```python
import jax
import jax.numpy as jnp
from jax import lax
from jax.sharding import PartitionSpec as P

N_CHUNKS = 2
LANE = 128


def select(rows, cols):
    return (rows[:, None] == cols[None, :]).astype(jnp.bfloat16)


def per_device(samples, basis, operators, cutouts, pixel_weights, detections, intersections):
    tiles_here, tile_cap, pixels = cutouts.shape
    coeff_dim = basis.shape[0]
    galaxy_count, sample_count, _unused = samples.shape
    sky_count = lax.axis_size("sky")
    expo_count = lax.axis_size("expo")
    send_cap = detections.shape[3]
    slot_count = sky_count * send_cap
    per_expo = sample_count // expo_count
    chunk_size = per_expo // N_CHUNKS
    chunk_samples = expo_count * chunk_size
    positions = tiles_here * tile_cap
    devices = expo_count * sky_count

    listed_all = lax.all_gather(
        detections.reshape(sky_count, send_cap), "expo", axis=0, tiled=False
    )
    sent_rows = lax.dynamic_index_in_dim(listed_all, lax.axis_index("expo"), 0, keepdims=False)
    listed_flat = listed_all.reshape(-1)
    onehot = (listed_flat[None, :] == jnp.arange(galaxy_count, dtype=jnp.int32)[:, None]).astype(
        jnp.float32
    )
    onehot_k = (
        onehot[:, None, :, None]
        * jnp.eye(chunk_size, dtype=jnp.float32)[None, :, None, :]
    ).reshape(galaxy_count * chunk_size, -1)

    arranged = samples.reshape(galaxy_count, expo_count, N_CHUNKS, chunk_size, coeff_dim)
    arranged = arranged.transpose(2, 1, 3, 0, 4).reshape(N_CHUNKS, chunk_samples, galaxy_count, -1)
    send_select = select(sent_rows.reshape(-1), jnp.arange(galaxy_count, dtype=jnp.int32))
    send_select = jnp.broadcast_to(send_select[None], (chunk_samples,) + send_select.shape)
    pick = jnp.maximum(intersections, 0).reshape(-1)
    pick_select = select(pick, jnp.arange(slot_count, dtype=jnp.int32))
    pick_select = jnp.broadcast_to(pick_select[None], (chunk_samples,) + pick_select.shape)
    live = intersections >= 0
    target = jnp.where(live, intersections, slot_count).reshape(-1)
    holder = jnp.full((slot_count,), positions, jnp.int32)
    holder = holder.at[target].set(jnp.arange(positions, dtype=jnp.int32), mode="drop")
    k_ids = jnp.arange(chunk_size, dtype=jnp.int32)
    back_src = (k_ids[None, :] * positions + holder[:, None]).reshape(-1)
    back_src = jnp.where(jnp.repeat(holder, chunk_size) < positions, back_src, -1)
    back_select = select(back_src, jnp.arange(chunk_size * positions, dtype=jnp.int32))
    back_select = jnp.broadcast_to(
        back_select.astype(jnp.float32)[None], (expo_count,) + back_select.shape
    )

    grad_pieces = []
    like_rows = []
    for chunk in range(N_CHUNKS):
        sent = lax.dot_general(
            send_select,
            arranged[chunk],
            (((2,), (1,)), ((0,), (0,))),
            preferred_element_type=jnp.float32,
        ).astype(jnp.bfloat16)
        sent = sent.transpose(1, 0, 2).reshape(-1, coeff_dim)
        incoming = lax.all_to_all(sent, "sky", split_axis=0, concat_axis=0, tiled=True)
        by_sample = incoming.reshape(slot_count, chunk_samples, coeff_dim).transpose(1, 0, 2)
        picked = lax.dot_general(
            pick_select,
            by_sample,
            (((2,), (1,)), ((0,), (0,))),
            preferred_element_type=jnp.float32,
        ).astype(jnp.bfloat16)
        picked = picked.reshape(chunk_samples, tiles_here, tile_cap, coeff_dim)
        picked = picked.transpose(1, 0, 2, 3).reshape(-1, coeff_dim)
        rendered = jnp.dot(picked, basis, preferred_element_type=jnp.float32).astype(jnp.bfloat16)
        rendered = rendered.reshape(tiles_here, chunk_samples * tile_cap, pixels)
        model = jnp.einsum("tnp,tpq->tnq", rendered, operators, preferred_element_type=jnp.float32)
        model = model.reshape(tiles_here, chunk_samples, tile_cap, pixels)
        resid = model - cutouts[:, None, :, :]
        weighted = pixel_weights[:, None, :, :] * resid
        pair_like = -0.5 / pixels * jnp.sum(weighted * resid, axis=-1)
        scaled = weighted.astype(jnp.bfloat16).reshape(tiles_here, chunk_samples * tile_cap, pixels)
        backed = jnp.einsum(
            "tnq,tpq->tnp", scaled, operators, preferred_element_type=jnp.float32
        ).astype(jnp.bfloat16)
        pair_grad = (
            -1.0
            / pixels
            * lax.dot_general(
                backed.reshape(-1, pixels),
                basis,
                (((1,), (1,)), ((), ())),
                preferred_element_type=jnp.float32,
            )
        )
        grad_src = pair_grad.reshape(tiles_here, expo_count, chunk_size, tile_cap, coeff_dim)
        grad_src = grad_src.transpose(1, 2, 0, 3, 4).reshape(expo_count, -1, coeff_dim)
        send_back = lax.dot_general(
            back_select,
            grad_src,
            (((2,), (1,)), ((0,), (0,))),
            precision=lax.Precision.HIGHEST,
            preferred_element_type=jnp.float32,
        ).reshape(-1, coeff_dim)
        back = lax.all_to_all(send_back, ("expo", "sky"), split_axis=0, concat_axis=0, tiled=True)
        grads = jnp.dot(onehot_k, back, precision=lax.Precision.HIGHEST)
        grad_pieces.append(grads.reshape(galaxy_count, chunk_size, coeff_dim))
        like_rows.append(
            pair_like.reshape(tiles_here, expo_count, chunk_size, tile_cap).transpose(1, 2, 0, 3)
        )
    likes = jnp.stack(like_rows, axis=1).reshape(expo_count, per_expo, positions)
    likes = jnp.take(likes, holder, axis=2, mode="fill", fill_value=0.0).transpose(0, 2, 1)
    like_width = send_cap * per_expo
    likes = likes.reshape(devices, like_width)
    likes = jnp.pad(likes, ((0, 0), (0, -like_width % LANE)))
    back_likes = lax.all_to_all(likes, ("expo", "sky"), split_axis=0, concat_axis=0, tiled=True)
    back_likes = back_likes[:, :like_width].reshape(-1, per_expo)
    like_out = jnp.dot(onehot, back_likes, precision=lax.Precision.HIGHEST)
    grad_out = jnp.concatenate(grad_pieces, axis=1)
    return (like_out, grad_out)


def solution(mesh):
    placed = (
        P("sky", None, None),
        P(),
        P(("expo", "sky"), None, None),
        P(("expo", "sky"), None, None),
        P(("expo", "sky"), None, None),
        P("expo", "sky", None, None),
        P(("expo", "sky"), None),
    )
    return jax.shard_map(
        per_device,
        mesh=mesh,
        in_specs=placed,
        out_specs=(P("sky", "expo"), P("sky", "expo", None)),
        check_vma=False,
    )
```

```python
import jax
import jax.numpy as jnp
from jax import lax
from jax.sharding import PartitionSpec as P

N_CHUNKS = 2
LANE = 128


def select(rows, cols):
    return (rows[:, None] == cols[None, :]).astype(jnp.bfloat16)


def per_device(samples, basis, operators, cutouts, pixel_weights, detections, intersections):
    tiles_here, tile_cap, pixels = cutouts.shape
    coeff_dim = basis.shape[0]
    galaxy_count, sample_count, _unused = samples.shape
    sky_count = lax.axis_size("sky")
    expo_count = lax.axis_size("expo")
    send_cap = detections.shape[3]
    slot_count = sky_count * send_cap
    per_expo = sample_count // expo_count
    chunk_size = per_expo // N_CHUNKS
    chunk_samples = expo_count * chunk_size
    positions = tiles_here * tile_cap
    devices = expo_count * sky_count

    listed_all = lax.all_gather(
        detections.reshape(sky_count, send_cap), "expo", axis=0, tiled=False
    )
    sent_rows = lax.dynamic_index_in_dim(listed_all, lax.axis_index("expo"), 0, keepdims=False)
    listed_flat = listed_all.reshape(-1)
    onehot = (listed_flat[None, :] == jnp.arange(galaxy_count, dtype=jnp.int32)[:, None]).astype(
        jnp.float32
    )
    onehot_k = (
        onehot[:, None, :, None]
        * jnp.eye(chunk_size, dtype=jnp.float32)[None, :, None, :]
    ).reshape(galaxy_count * chunk_size, -1)

    arranged = samples.reshape(galaxy_count, expo_count, N_CHUNKS, chunk_size, coeff_dim)
    arranged = arranged.transpose(2, 1, 3, 0, 4).reshape(N_CHUNKS, chunk_samples, galaxy_count, -1)
    send_select = select(sent_rows.reshape(-1), jnp.arange(galaxy_count, dtype=jnp.int32))
    send_select = jnp.broadcast_to(send_select[None], (chunk_samples,) + send_select.shape)
    pick = jnp.maximum(intersections, 0).reshape(-1)
    pick_select = select(pick, jnp.arange(slot_count, dtype=jnp.int32))
    pick_select = jnp.broadcast_to(pick_select[None], (chunk_samples,) + pick_select.shape)
    live = intersections >= 0
    target = jnp.where(live, intersections, slot_count).reshape(-1)
    holder = jnp.full((slot_count,), positions, jnp.int32)
    holder = holder.at[target].set(jnp.arange(positions, dtype=jnp.int32), mode="drop")
    k_ids = jnp.arange(chunk_size, dtype=jnp.int32)
    back_src = (k_ids[None, :] * positions + holder[:, None]).reshape(-1)
    back_src = jnp.where(jnp.repeat(holder, chunk_size) < positions, back_src, -1)
    back_select = select(back_src, jnp.arange(chunk_size * positions, dtype=jnp.int32))
    back_select = jnp.broadcast_to(
        back_select.astype(jnp.float32)[None], (expo_count,) + back_select.shape
    )

    grad_pieces = []
    like_rows = []
    for chunk in range(N_CHUNKS):
        sent = lax.dot_general(
            send_select,
            arranged[chunk],
            (((2,), (1,)), ((0,), (0,))),
            preferred_element_type=jnp.float32,
        ).astype(jnp.bfloat16)
        sent = sent.transpose(1, 0, 2).reshape(-1, coeff_dim)
        incoming = lax.all_to_all(sent, "sky", split_axis=0, concat_axis=0, tiled=True)
        by_sample = incoming.reshape(slot_count, chunk_samples, coeff_dim).transpose(1, 0, 2)
        picked = lax.dot_general(
            pick_select,
            by_sample,
            (((2,), (1,)), ((0,), (0,))),
            preferred_element_type=jnp.float32,
        ).astype(jnp.bfloat16)
        picked = picked.reshape(chunk_samples, tiles_here, tile_cap, coeff_dim)
        picked = picked.transpose(1, 0, 2, 3).reshape(-1, coeff_dim)
        rendered = jnp.dot(picked, basis, preferred_element_type=jnp.float32).astype(jnp.bfloat16)
        rendered = rendered.reshape(tiles_here, chunk_samples * tile_cap, pixels)
        model = jnp.einsum("tnp,tpq->tnq", rendered, operators, preferred_element_type=jnp.float32)
        model = model.reshape(tiles_here, chunk_samples, tile_cap, pixels)
        resid = model - cutouts[:, None, :, :]
        weighted = pixel_weights[:, None, :, :] * resid
        pair_like = -0.5 / pixels * jnp.sum(weighted * resid, axis=-1)
        scaled = weighted.astype(jnp.bfloat16).reshape(tiles_here, chunk_samples * tile_cap, pixels)
        backed = jnp.einsum(
            "tnq,tpq->tnp", scaled, operators, preferred_element_type=jnp.float32
        ).astype(jnp.bfloat16)
        pair_grad = (
            -1.0
            / pixels
            * lax.dot_general(
                backed.reshape(-1, pixels),
                basis,
                (((1,), (1,)), ((), ())),
                preferred_element_type=jnp.float32,
            )
        )
        grad_src = pair_grad.reshape(tiles_here, expo_count, chunk_size, tile_cap, coeff_dim)
        grad_src = grad_src.transpose(1, 2, 0, 3, 4).reshape(expo_count, -1, coeff_dim)
        send_back = lax.dot_general(
            back_select,
            grad_src,
            (((2,), (1,)), ((0,), (0,))),
            precision=lax.Precision.HIGH,
            preferred_element_type=jnp.float32,
        ).reshape(-1, coeff_dim)
        back = lax.all_to_all(send_back, ("expo", "sky"), split_axis=0, concat_axis=0, tiled=True)
        grads = jnp.dot(onehot_k, back, precision=lax.Precision.HIGH)
        grad_pieces.append(grads.reshape(galaxy_count, chunk_size, coeff_dim))
        like_rows.append(
            pair_like.reshape(tiles_here, expo_count, chunk_size, tile_cap).transpose(1, 2, 0, 3)
        )
    likes = jnp.stack(like_rows, axis=1).reshape(expo_count, per_expo, positions)
    likes = jnp.take(likes, holder, axis=2, mode="fill", fill_value=0.0).transpose(0, 2, 1)
    like_width = send_cap * per_expo
    likes = likes.reshape(devices, like_width)
    likes = jnp.pad(likes, ((0, 0), (0, -like_width % LANE)))
    back_likes = lax.all_to_all(likes, ("expo", "sky"), split_axis=0, concat_axis=0, tiled=True)
    back_likes = back_likes[:, :like_width].reshape(-1, per_expo)
    like_out = jnp.dot(onehot, back_likes, precision=lax.Precision.HIGHEST)
    grad_out = jnp.concatenate(grad_pieces, axis=1)
    return (like_out, grad_out)


def solution(mesh):
    placed = (
        P("sky", None, None),
        P(),
        P(("expo", "sky"), None, None),
        P(("expo", "sky"), None, None),
        P(("expo", "sky"), None, None),
        P("expo", "sky", None, None),
        P(("expo", "sky"), None),
    )
    return jax.shard_map(
        per_device,
        mesh=mesh,
        in_specs=placed,
        out_specs=(P("sky", "expo"), P("sky", "expo", None)),
        check_vma=False,
    )
```

```python
import jax
import jax.numpy as jnp
from jax import lax
from jax.sharding import PartitionSpec as P

N_CHUNKS = 2
LANE = 128


def select(rows, cols):
    return (rows[:, None] == cols[None, :]).astype(jnp.bfloat16)


def per_device(samples, basis, operators, cutouts, pixel_weights, detections, intersections):
    tiles_here, tile_cap, pixels = cutouts.shape
    coeff_dim = basis.shape[0]
    galaxy_count, sample_count, _unused = samples.shape
    sky_count = lax.axis_size("sky")
    expo_count = lax.axis_size("expo")
    send_cap = detections.shape[3]
    slot_count = sky_count * send_cap
    per_expo = sample_count // expo_count
    chunk_size = per_expo // N_CHUNKS
    chunk_samples = expo_count * chunk_size
    positions = tiles_here * tile_cap
    devices = expo_count * sky_count

    listed_all = lax.all_gather(
        detections.reshape(sky_count, send_cap), "expo", axis=0, tiled=False
    )
    sent_rows = lax.dynamic_index_in_dim(listed_all, lax.axis_index("expo"), 0, keepdims=False)
    listed_flat = listed_all.reshape(-1)
    onehot = (listed_flat[None, :] == jnp.arange(galaxy_count, dtype=jnp.int32)[:, None]).astype(
        jnp.float32
    )
    onehot_k = (
        onehot[:, None, :, None]
        * jnp.eye(chunk_size, dtype=jnp.float32)[None, :, None, :]
    ).reshape(galaxy_count * chunk_size, -1)

    arranged = samples.reshape(galaxy_count, expo_count, N_CHUNKS, chunk_size, coeff_dim)
    arranged = arranged.transpose(2, 1, 3, 0, 4).reshape(N_CHUNKS, chunk_samples, galaxy_count, -1)
    send_select = select(sent_rows.reshape(-1), jnp.arange(galaxy_count, dtype=jnp.int32))
    send_select = jnp.broadcast_to(send_select[None], (chunk_samples,) + send_select.shape)
    pick = jnp.maximum(intersections, 0).reshape(-1)
    pick_select = select(pick, jnp.arange(slot_count, dtype=jnp.int32))
    pick_select = jnp.broadcast_to(pick_select[None], (chunk_samples,) + pick_select.shape)
    live = intersections >= 0
    target = jnp.where(live, intersections, slot_count).reshape(-1)
    holder = jnp.full((slot_count,), positions, jnp.int32)
    holder = holder.at[target].set(jnp.arange(positions, dtype=jnp.int32), mode="drop")
    k_ids = jnp.arange(chunk_size, dtype=jnp.int32)
    back_src = (k_ids[None, :] * positions + holder[:, None]).reshape(-1)
    back_src = jnp.where(jnp.repeat(holder, chunk_size) < positions, back_src, -1)
    back_select = select(back_src, jnp.arange(chunk_size * positions, dtype=jnp.int32))
    back_select = jnp.broadcast_to(
        back_select.astype(jnp.float32)[None], (expo_count,) + back_select.shape
    )

    grad_pieces = []
    like_rows = []
    for chunk in range(N_CHUNKS):
        sent = lax.dot_general(
            send_select,
            arranged[chunk],
            (((2,), (1,)), ((0,), (0,))),
            preferred_element_type=jnp.float32,
        ).astype(jnp.bfloat16)
        sent = sent.transpose(1, 0, 2).reshape(-1, coeff_dim)
        incoming = lax.all_to_all(sent, "sky", split_axis=0, concat_axis=0, tiled=True)
        by_sample = incoming.reshape(slot_count, chunk_samples, coeff_dim).transpose(1, 0, 2)
        picked = lax.dot_general(
            pick_select,
            by_sample,
            (((2,), (1,)), ((0,), (0,))),
            preferred_element_type=jnp.float32,
        ).astype(jnp.bfloat16)
        picked = picked.reshape(chunk_samples, tiles_here, tile_cap, coeff_dim)
        picked = picked.transpose(1, 0, 2, 3).reshape(-1, coeff_dim)
        rendered = jnp.dot(picked, basis, preferred_element_type=jnp.float32).astype(jnp.bfloat16)
        rendered = rendered.reshape(tiles_here, chunk_samples * tile_cap, pixels)
        model = jnp.einsum("tnp,tpq->tnq", rendered, operators, preferred_element_type=jnp.float32)
        model = model.reshape(tiles_here, chunk_samples, tile_cap, pixels)
        resid = model - cutouts[:, None, :, :]
        weighted = pixel_weights[:, None, :, :] * resid
        pair_like = -0.5 / pixels * jnp.sum(weighted * resid, axis=-1)
        scaled = weighted.astype(jnp.bfloat16).reshape(tiles_here, chunk_samples * tile_cap, pixels)
        backed = jnp.einsum(
            "tnq,tpq->tnp", scaled, operators, preferred_element_type=jnp.float32
        ).astype(jnp.bfloat16)
        pair_grad = (
            -1.0
            / pixels
            * lax.dot_general(
                backed.reshape(-1, pixels),
                basis,
                (((1,), (1,)), ((), ())),
                preferred_element_type=jnp.float32,
            )
        )
        grad_src = pair_grad.reshape(tiles_here, expo_count, chunk_size, tile_cap, coeff_dim)
        grad_src = grad_src.transpose(1, 2, 0, 3, 4).reshape(expo_count, -1, coeff_dim)
        send_back = lax.dot_general(
            back_select,
            grad_src,
            (((2,), (1,)), ((0,), (0,))),
            precision=lax.Precision.HIGH,
            preferred_element_type=jnp.float32,
        ).reshape(-1, coeff_dim)
        back = lax.all_to_all(send_back, ("expo", "sky"), split_axis=0, concat_axis=0, tiled=True)
        grads = jnp.dot(onehot_k, back, precision=lax.Precision.HIGH)
        grad_pieces.append(grads.reshape(galaxy_count, chunk_size, coeff_dim))
        like_rows.append(
            pair_like.reshape(tiles_here, expo_count, chunk_size, tile_cap).transpose(1, 2, 0, 3)
        )
    likes = jnp.stack(like_rows, axis=1).reshape(expo_count, per_expo, positions)
    likes = jnp.take(likes, holder, axis=2, mode="fill", fill_value=0.0).transpose(0, 2, 1)
    like_width = send_cap * per_expo
    likes = likes.reshape(devices, like_width)
    likes = jnp.pad(likes, ((0, 0), (0, -like_width % LANE)))
    back_likes = lax.all_to_all(likes, ("expo", "sky"), split_axis=0, concat_axis=0, tiled=True)
    back_likes = back_likes[:, :like_width].reshape(-1, per_expo)
    like_out = jnp.dot(onehot, back_likes, precision=lax.Precision.HIGH)
    grad_out = jnp.concatenate(grad_pieces, axis=1)
    return (like_out, grad_out)


def solution(mesh):
    placed = (
        P("sky", None, None),
        P(),
        P(("expo", "sky"), None, None),
        P(("expo", "sky"), None, None),
        P(("expo", "sky"), None, None),
        P("expo", "sky", None, None),
        P(("expo", "sky"), None),
    )
    return jax.shard_map(
        per_device,
        mesh=mesh,
        in_specs=placed,
        out_specs=(P("sky", "expo"), P("sky", "expo", None)),
        check_vma=False,
    )
```

```python
import jax
import jax.numpy as jnp
from jax import lax
from jax.sharding import PartitionSpec as P

N_CHUNKS = 2
LANE = 128


def select(rows, cols):
    return (rows[:, None] == cols[None, :]).astype(jnp.bfloat16)


def per_device(samples, basis, operators, cutouts, pixel_weights, detections, intersections):
    tiles_here, tile_cap, pixels = cutouts.shape
    coeff_dim = basis.shape[0]
    galaxy_count, sample_count, _unused = samples.shape
    sky_count = lax.axis_size("sky")
    expo_count = lax.axis_size("expo")
    send_cap = detections.shape[3]
    slot_count = sky_count * send_cap
    per_expo = sample_count // expo_count
    chunk_size = per_expo // N_CHUNKS
    chunk_samples = expo_count * chunk_size
    positions = tiles_here * tile_cap
    devices = expo_count * sky_count

    listed_all = lax.all_gather(
        detections.reshape(sky_count, send_cap), "expo", axis=0, tiled=False
    )
    sent_rows = lax.dynamic_index_in_dim(listed_all, lax.axis_index("expo"), 0, keepdims=False)
    listed_flat = listed_all.reshape(-1)
    onehot = (listed_flat[None, :] == jnp.arange(galaxy_count, dtype=jnp.int32)[:, None]).astype(
        jnp.float32
    )
    onehot_k = (
        onehot[:, None, :, None]
        * jnp.eye(chunk_size, dtype=jnp.float32)[None, :, None, :]
    ).reshape(galaxy_count * chunk_size, -1)

    arranged = samples.reshape(galaxy_count, expo_count, N_CHUNKS, chunk_size, coeff_dim)
    arranged = arranged.transpose(2, 1, 3, 0, 4).reshape(N_CHUNKS, chunk_samples, galaxy_count, -1)
    send_select = select(sent_rows.reshape(-1), jnp.arange(galaxy_count, dtype=jnp.int32))
    send_select = jnp.broadcast_to(send_select[None], (chunk_samples,) + send_select.shape)
    pick = jnp.maximum(intersections, 0).reshape(-1)
    pick_select = select(pick, jnp.arange(slot_count, dtype=jnp.int32))
    pick_select = jnp.broadcast_to(pick_select[None], (chunk_samples,) + pick_select.shape)
    live = intersections >= 0
    target = jnp.where(live, intersections, slot_count).reshape(-1)
    holder = jnp.full((slot_count,), positions, jnp.int32)
    holder = holder.at[target].set(jnp.arange(positions, dtype=jnp.int32), mode="drop")
    k_ids = jnp.arange(chunk_size, dtype=jnp.int32)
    back_src = (k_ids[None, :] * positions + holder[:, None]).reshape(-1)
    back_src = jnp.where(jnp.repeat(holder, chunk_size) < positions, back_src, -1)
    back_select = select(back_src, jnp.arange(chunk_size * positions, dtype=jnp.int32))
    back_select = jnp.broadcast_to(
        back_select.astype(jnp.float32)[None], (expo_count,) + back_select.shape
    )

    def forward(chunk):
        sent = lax.dot_general(
            send_select,
            arranged[chunk],
            (((2,), (1,)), ((0,), (0,))),
            preferred_element_type=jnp.float32,
        ).astype(jnp.bfloat16)
        return sent.transpose(1, 0, 2).reshape(-1, coeff_dim)

    early = []
    grad_pieces = []
    like_rows = []
    for chunk in range(N_CHUNKS):
        incoming = early.pop() if early else lax.all_to_all(
            forward(chunk), "sky", split_axis=0, concat_axis=0, tiled=True
        )
        by_sample = incoming.reshape(slot_count, chunk_samples, coeff_dim).transpose(1, 0, 2)
        picked = lax.dot_general(
            pick_select,
            by_sample,
            (((2,), (1,)), ((0,), (0,))),
            preferred_element_type=jnp.float32,
        ).astype(jnp.bfloat16)
        picked = picked.reshape(chunk_samples, tiles_here, tile_cap, coeff_dim)
        picked = picked.transpose(1, 0, 2, 3).reshape(-1, coeff_dim)
        rendered = jnp.dot(picked, basis, preferred_element_type=jnp.float32).astype(jnp.bfloat16)
        rendered = rendered.reshape(tiles_here, chunk_samples * tile_cap, pixels)
        model = jnp.einsum("tnp,tpq->tnq", rendered, operators, preferred_element_type=jnp.float32)
        if chunk + 1 < N_CHUNKS:
            model, sent = lax.optimization_barrier((model, forward(chunk + 1)))
            early.append(lax.all_to_all(sent, "sky", split_axis=0, concat_axis=0, tiled=True))
        model = model.reshape(tiles_here, chunk_samples, tile_cap, pixels)
        resid = model - cutouts[:, None, :, :]
        weighted = pixel_weights[:, None, :, :] * resid
        pair_like = -0.5 / pixels * jnp.sum(weighted * resid, axis=-1)
        scaled = weighted.astype(jnp.bfloat16).reshape(tiles_here, chunk_samples * tile_cap, pixels)
        backed = jnp.einsum(
            "tnq,tpq->tnp", scaled, operators, preferred_element_type=jnp.float32
        ).astype(jnp.bfloat16)
        pair_grad = (
            -1.0
            / pixels
            * lax.dot_general(
                backed.reshape(-1, pixels),
                basis,
                (((1,), (1,)), ((), ())),
                preferred_element_type=jnp.float32,
            )
        )
        grad_src = pair_grad.reshape(tiles_here, expo_count, chunk_size, tile_cap, coeff_dim)
        grad_src = grad_src.transpose(1, 2, 0, 3, 4).reshape(expo_count, -1, coeff_dim)
        send_back = lax.dot_general(
            back_select,
            grad_src,
            (((2,), (1,)), ((0,), (0,))),
            precision=lax.Precision.HIGH,
            preferred_element_type=jnp.float32,
        ).reshape(-1, coeff_dim)
        back = lax.all_to_all(send_back, ("expo", "sky"), split_axis=0, concat_axis=0, tiled=True)
        grads = jnp.dot(onehot_k, back, precision=lax.Precision.HIGH)
        grad_pieces.append(grads.reshape(galaxy_count, chunk_size, coeff_dim))
        like_rows.append(
            pair_like.reshape(tiles_here, expo_count, chunk_size, tile_cap).transpose(1, 2, 0, 3)
        )
    likes = jnp.stack(like_rows, axis=1).reshape(expo_count, per_expo, positions)
    likes = jnp.take(likes, holder, axis=2, mode="fill", fill_value=0.0).transpose(0, 2, 1)
    like_width = send_cap * per_expo
    likes = likes.reshape(devices, like_width)
    likes = jnp.pad(likes, ((0, 0), (0, -like_width % LANE)))
    back_likes = lax.all_to_all(likes, ("expo", "sky"), split_axis=0, concat_axis=0, tiled=True)
    back_likes = back_likes[:, :like_width].reshape(-1, per_expo)
    like_out = jnp.dot(onehot, back_likes, precision=lax.Precision.HIGH)
    grad_out = jnp.concatenate(grad_pieces, axis=1)
    return (like_out, grad_out)


def solution(mesh):
    placed = (
        P("sky", None, None),
        P(),
        P(("expo", "sky"), None, None),
        P(("expo", "sky"), None, None),
        P(("expo", "sky"), None, None),
        P("expo", "sky", None, None),
        P(("expo", "sky"), None),
    )
    return jax.shard_map(
        per_device,
        mesh=mesh,
        in_specs=placed,
        out_specs=(P("sky", "expo"), P("sky", "expo", None)),
        check_vma=False,
    )
```
